256 devices in a mesh: ax: 32 (over y, z_hi, core), rad: 8 (over z_lo, x).
Axes of the slice: x: 4, y: 4, z: 8 (z_hi: 4, z_lo: 2; z = z_hi * 2 + z_lo), core: 2. Of those that a mesh axis runs over, the one named last changes fastest.
Arguments:
- state: float32 [512, 256, 5, 384], P('ax', 'rad'), may hold values from -6 to 6
- metric: float32 [512, 256, 384], P('ax', 'rad'), may hold values from 0.25 to 4
- deriv: float32 [512, 512], replicated, may hold values from -0.25 to 0.25
- filt_corr: float32 [512, 512], replicated, may hold values from -0.25 to 0.25
- jac_axial: float32 [5, 5], replicated, may hold values from -3 to 3
- jac_radial: float32 [5, 5], replicated, may hold values from -3 to 3
Outputs:
- advanced: float32 [512, 256, 5, 384], P('ax', 'rad')
The draws below stay inside these ranges and needn't reach their ends.
All inputs are finite; a program needn't handle non-finite values.
Results may differ from the reference program's by a relative error of at most 0.000084.
Values sent between devices are 32-bit elements; how exact they have to be, the bound alone decides.
No kernel may reach another device: no remote copies, remote signals or barrier semaphores. Data moves between devices by JAX's collectives and lax.ppermute only.
A program may use at most 128 MiB of HBM per device.

```python
import math
import jax
import jax.numpy as jnp
from jax import lax

NX = 512
VARS = 5
NAZ = 384
NR = 256


def levels(stream_key, dims, cuts, least, largest):
    def one(position, shards_of):
        draws = jax.random.uniform(jax.random.fold_in(jax.random.fold_in(stream_key, 6), position), (shards_of,), jnp.float32, least / len(cuts), largest / len(cuts))
        return jnp.repeat(jnp.exp(draws), dims[position] // shards_of).reshape((-1,) + (1,) * (len(dims) - position - 1))

    factor_of = one(*cuts[0])
    for cut in cuts[1:]:
        factor_of = factor_of * one(*cut)
    return factor_of


def noise(stream_key, extent, scale, reach, cuts=(), held_as=jnp.bfloat16):
    array = scale * jax.random.normal(stream_key, extent, jnp.float32)
    if cuts:
        array = array * levels(stream_key, extent, cuts, -0.22, 0.18)
    return jnp.clip(array, -reach, reach).astype(held_as)


def setup_inputs(seed: int = 0) -> dict:
    streams_of = jax.random.split(jax.random.key(seed), 7)
    return {
        "state": noise(streams_of[0], (NX, NR, VARS, NAZ), 1.0, 6.0, ((0, 32), (1, 8)), jnp.float32),
        "metric": jnp.clip(jnp.exp(math.log(4.0) - 2.7725887 * jax.random.uniform(streams_of[1], (NX, NR, NAZ), jnp.float32) ** levels(streams_of[1], (NX, NR, NAZ), ((0, 32), (1, 8)), -0.2, 0.2)), 0.25, 4.0),
        "deriv": noise(streams_of[2], (NX, NX), NX ** -0.5, 0.25, (), jnp.float32),
        "filt_corr": noise(streams_of[3], (NX, NX), NX ** -0.5, 0.25, (), jnp.float32),
        "jac_axial": noise(streams_of[4], (VARS, VARS), 0.5, 3.0, (), jnp.float32),
        "jac_radial": noise(streams_of[5], (VARS, VARS), 0.5, 3.0, (), jnp.float32),
    }


section_step = 0.25
viscosity = 0.5


def axial_viscous(padded):
    field = padded[:, :, :5]
    weight = padded[:, :, 5:]
    centre = field[1:-1]
    upper = 0.5 * (weight[1:-1] + weight[2:])
    lower = 0.5 * (weight[1:-1] + weight[:-2])
    return upper * (field[2:] - centre) - lower * (centre - field[:-2])


def radial_terms(padded, jac_radial):
    field = padded[:, :, :5]
    weight = padded[:, :, 5:]
    centre = field[:, 1:-1]
    upper = 0.5 * (weight[:, 1:-1] + weight[:, 2:])
    lower = 0.5 * (weight[:, 1:-1] + weight[:, :-2])
    flux = upper * (field[:, 2:] - centre) - lower * (centre - field[:, :-2])
    spread = 0.5 * (field[:, 2:] - field[:, :-2])
    mixed = jnp.einsum("xrka,kv->xrva", spread, jac_radial, precision=lax.Precision.HIGHEST)
    return mixed + viscosity * flux


def column_section(state, weight, deriv, filt_corr, jac_axial, jac_radial):
    flat = state.reshape(state.shape[0], -1)
    slope = jnp.dot(deriv, flat, precision=lax.Precision.HIGHEST, preferred_element_type=jnp.float32).reshape(state.shape)
    smooth = jnp.dot(filt_corr, flat, precision=lax.Precision.HIGHEST, preferred_element_type=jnp.float32).reshape(state.shape)
    mixed = jnp.einsum("xrka,kv->xrva", slope, jac_axial, precision=lax.Precision.HIGHEST)
    packed = jnp.concatenate([state, weight], axis=2)
    padded = jnp.pad(packed, ((1, 1), (1, 1), (0, 0), (0, 0)))
    total = viscosity * axial_viscous(padded[:, 1:-1]) + radial_terms(padded[1:-1], jac_radial)
    return state - smooth + section_step * (mixed + total)


def reference(state, metric, deriv, filt_corr, jac_axial, jac_radial):
    blocks = NAZ // 32
    pieces = jnp.moveaxis(state.reshape(NX, NR, VARS, blocks, 32), 3, 0)
    weights = jnp.moveaxis(metric.reshape(NX, NR, 1, blocks, 32), 3, 0)

    def one_block(pair):
        return column_section(pair[0], pair[1], deriv, filt_corr, jac_axial, jac_radial)

    result = lax.map(one_block, (pieces, weights))
    return jnp.moveaxis(result, 0, 3).reshape(NX, NR, VARS, NAZ)
```

```python
import functools

import jax
import jax.numpy as jnp
from jax import lax
from jax.experimental import pallas as pl
from jax.experimental.pallas import tpu as pltpu
from jax.sharding import PartitionSpec as P

section_step = 0.25
viscosity = 0.5
CHUNK = 128


def extended(x, sides, width):
    for axis, dim in sides:
        peers, length = (lax.axis_size(axis), x.shape[dim])
        up = [(i, (i + 1) % peers) for i in range(peers - 1)]
        down = [(j, i) for i, j in up]
        last = lax.slice_in_dim(x, length - width, length, axis=dim)
        leading = lax.slice_in_dim(x, 0, width, axis=dim)
        before = lax.ppermute(last, axis, up)
        after = lax.ppermute(leading, axis, down)
        x = jnp.concatenate([before, x, after], axis=dim)
    return x


def axial_viscous(padded):
    field = padded[:, :, :5]
    weight = padded[:, :, 5:]
    centre = field[1:-1]
    upper = 0.5 * (weight[1:-1] + weight[2:])
    lower = 0.5 * (weight[1:-1] + weight[:-2])
    return upper * (field[2:] - centre) - lower * (centre - field[:-2])


def radial_terms(padded, jac_radial):
    field = padded[:, :, :5]
    weight = padded[:, :, 5:]
    centre = field[:, 1:-1]
    upper = 0.5 * (weight[:, 1:-1] + weight[:, 2:])
    lower = 0.5 * (weight[:, 1:-1] + weight[:, :-2])
    flux = upper * (field[:, 2:] - centre) - lower * (centre - field[:, :-2])
    spread = 0.5 * (field[:, 2:] - field[:, :-2])
    mixed = jnp.einsum("xrka,kv->xrva", spread, jac_radial, precision=lax.Precision.HIGHEST)
    return mixed + viscosity * flux


def line_kernel(jac_ref, lines_ref, mats_ref, out_ref):
    S, V, XL, C = lines_ref.shape
    nx = S * XL
    cols = [lines_ref[:, v, :, :].reshape(nx, C) for v in range(V)]
    wide = jnp.concatenate(cols, axis=1)
    prod = jnp.dot(
        mats_ref[...], wide, precision=lax.Precision.HIGHEST, preferred_element_type=jnp.float32
    )
    smooth = prod[:nx]
    slope = prod[nx:]
    for v in range(V):
        mix = jac_ref[0, v] * slope[:, 0:C]
        for k in range(1, V):
            mix = mix + jac_ref[k, v] * slope[:, k * C:(k + 1) * C]
        res = cols[v] - smooth[:, v * C:(v + 1) * C] + section_step * mix
        out_ref[:, v, :, :] = res.reshape(S, XL, C)


def line_section(lines, mats, jac_axial):
    S, V, XL, C = lines.shape
    return pl.pallas_call(
        line_kernel,
        out_shape=jax.ShapeDtypeStruct(lines.shape, lines.dtype),
        in_specs=[
            pl.BlockSpec(memory_space=pltpu.SMEM),
            pl.BlockSpec(memory_space=pltpu.VMEM),
            pl.BlockSpec(memory_space=pltpu.VMEM),
        ],
        out_specs=pl.BlockSpec(memory_space=pltpu.VMEM),
        compiler_params=pltpu.CompilerParams(vmem_limit_bytes=48 * 1024 * 1024),
    )(jac_axial, lines, mats)


def body(state, metric, deriv, filt_corr, jac_axial, jac_radial):
    nx, nr, nv, na = state.shape
    peers = lax.axis_size("ax")
    assert nr == peers
    mats = jnp.concatenate([filt_corr, deriv], axis=0)
    send = jnp.transpose(state, (1, 2, 0, 3))
    chunk = CHUNK if na % CHUNK == 0 else na
    rets = []
    for c in range(na // chunk):
        piece = send[:, :, :, c * chunk:(c + 1) * chunk]
        lines = lax.all_to_all(piece, "ax", split_axis=0, concat_axis=0, tiled=True)
        res = line_section(lines, mats, jac_axial)
        rets.append(lax.all_to_all(res, "ax", split_axis=0, concat_axis=0, tiled=True))
    ret = jnp.concatenate(rets, axis=3)
    weight = metric.reshape(metric.shape[0], metric.shape[1], 1, metric.shape[2])
    packed = jnp.concatenate([state, weight], axis=2)
    padded = extended(packed, (("ax", 0), ("rad", 1)), 1)
    local = viscosity * axial_viscous(padded[:, 1:-1]) + radial_terms(padded[1:-1], jac_radial)
    return jnp.transpose(ret, (2, 0, 1, 3)) + section_step * local


def solution(mesh):
    in_specs = (P("ax", "rad", None, None), P("ax", "rad", None), P(), P(), P(), P())
    out_specs = P("ax", "rad", None, None)
    return jax.shard_map(body, mesh=mesh, in_specs=in_specs, out_specs=out_specs, check_vma=False)
```

```python
import functools

import jax
import jax.numpy as jnp
from jax import lax
from jax.experimental import pallas as pl
from jax.experimental.pallas import tpu as pltpu
from jax.sharding import PartitionSpec as P

section_step = 0.25
viscosity = 0.5


def extended(x, sides, width):
    for axis, dim in sides:
        peers, length = (lax.axis_size(axis), x.shape[dim])
        up = [(i, (i + 1) % peers) for i in range(peers - 1)]
        down = [(j, i) for i, j in up]
        last = lax.slice_in_dim(x, length - width, length, axis=dim)
        leading = lax.slice_in_dim(x, 0, width, axis=dim)
        before = lax.ppermute(last, axis, up)
        after = lax.ppermute(leading, axis, down)
        x = jnp.concatenate([before, x, after], axis=dim)
    return x


def axial_viscous(padded):
    field = padded[:, :, :5]
    weight = padded[:, :, 5:]
    centre = field[1:-1]
    upper = 0.5 * (weight[1:-1] + weight[2:])
    lower = 0.5 * (weight[1:-1] + weight[:-2])
    return upper * (field[2:] - centre) - lower * (centre - field[:-2])


def radial_terms(padded, jac_radial):
    field = padded[:, :, :5]
    weight = padded[:, :, 5:]
    centre = field[:, 1:-1]
    upper = 0.5 * (weight[:, 1:-1] + weight[:, 2:])
    lower = 0.5 * (weight[:, 1:-1] + weight[:, :-2])
    flux = upper * (field[:, 2:] - centre) - lower * (centre - field[:, :-2])
    spread = 0.5 * (field[:, 2:] - field[:, :-2])
    nv = spread.shape[2]
    mixed = []
    for v in range(nv):
        acc = jac_radial[0, v] * spread[:, :, 0]
        for k in range(1, nv):
            acc = acc + jac_radial[k, v] * spread[:, :, k]
        mixed.append(acc)
    return jnp.stack(mixed, axis=2) + viscosity * flux


def line_kernel(jac_ref, lines_ref, mats_ref, out_ref):
    S, V, XL, C = lines_ref.shape
    nx = S * XL
    cols = [lines_ref[:, v, :, :].reshape(nx, C) for v in range(V)]
    wide = jnp.concatenate(cols, axis=1)
    prod = jnp.dot(
        mats_ref[...], wide, precision=lax.Precision.HIGHEST, preferred_element_type=jnp.float32
    )
    smooth = prod[:nx]
    slope = prod[nx:]
    for v in range(V):
        mix = jac_ref[0, v] * slope[:, 0:C]
        for k in range(1, V):
            mix = mix + jac_ref[k, v] * slope[:, k * C:(k + 1) * C]
        res = cols[v] - smooth[:, v * C:(v + 1) * C] + section_step * mix
        out_ref[:, v, :, :] = res.reshape(S, XL, C)


def line_section(lines, mats, jac_axial):
    S, V, XL, C = lines.shape
    return pl.pallas_call(
        line_kernel,
        out_shape=jax.ShapeDtypeStruct(lines.shape, lines.dtype),
        in_specs=[
            pl.BlockSpec(memory_space=pltpu.SMEM),
            pl.BlockSpec(memory_space=pltpu.VMEM),
            pl.BlockSpec(memory_space=pltpu.VMEM),
        ],
        out_specs=pl.BlockSpec(memory_space=pltpu.VMEM),
        compiler_params=pltpu.CompilerParams(vmem_limit_bytes=48 * 1024 * 1024),
    )(jac_axial, lines, mats)


def body(state, metric, deriv, filt_corr, jac_axial, jac_radial):
    nx, nr, nv, na = state.shape
    peers = lax.axis_size("ax")
    assert nr == peers
    mats = jnp.concatenate([filt_corr, deriv], axis=0)
    send = jnp.transpose(state, (1, 2, 0, 3))
    lines = lax.all_to_all(send, "ax", split_axis=0, concat_axis=0, tiled=True)
    weight = metric.reshape(metric.shape[0], metric.shape[1], 1, metric.shape[2])
    packed = jnp.concatenate([state, weight], axis=2)
    padded = extended(packed, (("ax", 0), ("rad", 1)), 1)
    local = viscosity * axial_viscous(padded[:, 1:-1]) + radial_terms(padded[1:-1], jac_radial)
    lines, local = lax.optimization_barrier((lines, local))
    res = line_section(lines, mats, jac_axial)
    ret = lax.all_to_all(res, "ax", split_axis=0, concat_axis=0, tiled=True)
    return jnp.transpose(ret, (2, 0, 1, 3)) + section_step * local


def solution(mesh):
    in_specs = (P("ax", "rad", None, None), P("ax", "rad", None), P(), P(), P(), P())
    out_specs = P("ax", "rad", None, None)
    return jax.shard_map(body, mesh=mesh, in_specs=in_specs, out_specs=out_specs, check_vma=False)
```

```python
import functools

import jax
import jax.numpy as jnp
from jax import lax
from jax.experimental import pallas as pl
from jax.experimental.pallas import tpu as pltpu
from jax.sharding import PartitionSpec as P

section_step = 0.25
viscosity = 0.5
CHUNK = 128


def extended(x, sides, width):
    for axis, dim in sides:
        peers, length = (lax.axis_size(axis), x.shape[dim])
        up = [(i, (i + 1) % peers) for i in range(peers - 1)]
        down = [(j, i) for i, j in up]
        last = lax.slice_in_dim(x, length - width, length, axis=dim)
        leading = lax.slice_in_dim(x, 0, width, axis=dim)
        before = lax.ppermute(last, axis, up)
        after = lax.ppermute(leading, axis, down)
        x = jnp.concatenate([before, x, after], axis=dim)
    return x


def axial_viscous(padded):
    field = padded[:, :, :5]
    weight = padded[:, :, 5:]
    centre = field[1:-1]
    upper = 0.5 * (weight[1:-1] + weight[2:])
    lower = 0.5 * (weight[1:-1] + weight[:-2])
    return upper * (field[2:] - centre) - lower * (centre - field[:-2])


def radial_terms(padded, jac_radial):
    field = padded[:, :, :5]
    weight = padded[:, :, 5:]
    centre = field[:, 1:-1]
    upper = 0.5 * (weight[:, 1:-1] + weight[:, 2:])
    lower = 0.5 * (weight[:, 1:-1] + weight[:, :-2])
    flux = upper * (field[:, 2:] - centre) - lower * (centre - field[:, :-2])
    spread = 0.5 * (field[:, 2:] - field[:, :-2])
    nv = spread.shape[2]
    mixed = []
    for v in range(nv):
        acc = jac_radial[0, v] * spread[:, :, 0]
        for k in range(1, nv):
            acc = acc + jac_radial[k, v] * spread[:, :, k]
        mixed.append(acc)
    return jnp.stack(mixed, axis=2) + viscosity * flux


def line_kernel(jac_ref, lines_ref, mats_ref, out_ref):
    S, V, XL, C = lines_ref.shape
    nx = S * XL
    cols = [lines_ref[:, v, :, :].reshape(nx, C) for v in range(V)]
    wide = jnp.concatenate(cols, axis=1)
    prod = jnp.dot(
        mats_ref[...], wide, precision=lax.Precision.HIGHEST, preferred_element_type=jnp.float32
    )
    smooth = prod[:nx]
    slope = prod[nx:]
    for v in range(V):
        mix = jac_ref[0, v] * slope[:, 0:C]
        for k in range(1, V):
            mix = mix + jac_ref[k, v] * slope[:, k * C:(k + 1) * C]
        res = cols[v] - smooth[:, v * C:(v + 1) * C] + section_step * mix
        out_ref[:, v, :, :] = res.reshape(S, XL, C)


def line_section(lines, mats, jac_axial):
    S, V, XL, C = lines.shape
    return pl.pallas_call(
        line_kernel,
        out_shape=jax.ShapeDtypeStruct(lines.shape, lines.dtype),
        in_specs=[
            pl.BlockSpec(memory_space=pltpu.SMEM),
            pl.BlockSpec(memory_space=pltpu.VMEM),
            pl.BlockSpec(memory_space=pltpu.VMEM),
        ],
        out_specs=pl.BlockSpec(memory_space=pltpu.VMEM),
        compiler_params=pltpu.CompilerParams(vmem_limit_bytes=48 * 1024 * 1024),
    )(jac_axial, lines, mats)


def body(state, metric, deriv, filt_corr, jac_axial, jac_radial):
    nx, nr, nv, na = state.shape
    peers = lax.axis_size("ax")
    assert nr == peers
    mats = jnp.concatenate([filt_corr, deriv], axis=0)
    send = jnp.transpose(state, (1, 2, 0, 3))
    chunk = CHUNK if na % CHUNK == 0 else na
    count = na // chunk

    def exchange(x):
        return lax.all_to_all(x, "ax", split_axis=0, concat_axis=0, tiled=True)

    lines = [exchange(send[..., c * chunk:(c + 1) * chunk]) for c in range(count)]
    weight = metric.reshape(metric.shape[0], metric.shape[1], 1, metric.shape[2])
    packed = jnp.concatenate([state, weight], axis=2)
    padded = extended(packed, (("ax", 0), ("rad", 1)), 1)
    local = viscosity * axial_viscous(padded[:, 1:-1]) + radial_terms(padded[1:-1], jac_radial)
    res = [line_section(lines[0], mats, jac_axial)]
    for c in range(1, count):
        nxt, prev = lax.optimization_barrier((lines[c], res[-1]))
        res[-1] = prev
        res.append(line_section(nxt, mats, jac_axial))
    rets = [exchange(res[0])]
    for c in range(1, count):
        prev, cur = lax.optimization_barrier((rets[-1], res[c]))
        rets[-1] = prev
        rets.append(exchange(cur))
    ret = jnp.concatenate(rets, axis=3)
    return jnp.transpose(ret, (2, 0, 1, 3)) + section_step * local


def solution(mesh):
    in_specs = (P("ax", "rad", None, None), P("ax", "rad", None), P(), P(), P(), P())
    out_specs = P("ax", "rad", None, None)
    return jax.shard_map(body, mesh=mesh, in_specs=in_specs, out_specs=out_specs, check_vma=False)
```

```python
import functools

import jax
import jax.numpy as jnp
from jax import lax
from jax.experimental import pallas as pl
from jax.experimental.pallas import tpu as pltpu
from jax.sharding import PartitionSpec as P

section_step = 0.25
viscosity = 0.5


def halos(x, axis, dim):
    peers, length = (lax.axis_size(axis), x.shape[dim])
    up = [(i, (i + 1) % peers) for i in range(peers - 1)]
    down = [(j, i) for i, j in up]
    last = lax.slice_in_dim(x, length - 1, length, axis=dim)
    leading = lax.slice_in_dim(x, 0, 1, axis=dim)
    return lax.ppermute(last, axis, up), lax.ppermute(leading, axis, down)


def viscous(field, weight, before, after, wbefore, wafter, dim):
    up_f = jnp.concatenate([lax.slice_in_dim(field, 1, field.shape[dim], axis=dim), after], axis=dim)
    dn_f = jnp.concatenate([before, lax.slice_in_dim(field, 0, field.shape[dim] - 1, axis=dim)], axis=dim)
    up_w = jnp.concatenate([lax.slice_in_dim(weight, 1, weight.shape[dim], axis=dim), wafter], axis=dim)
    dn_w = jnp.concatenate([wbefore, lax.slice_in_dim(weight, 0, weight.shape[dim] - 1, axis=dim)], axis=dim)
    upper = 0.5 * (weight + up_w)
    lower = 0.5 * (weight + dn_w)
    return upper * (up_f - field) - lower * (field - dn_f), up_f, dn_f


def stencil(state, weight, ax_halo, rad_halo, jac_radial):
    nv = state.shape[2]
    (xb, xa), (rb, ra) = ax_halo, rad_halo
    visc_ax, _, _ = viscous(state, weight, xb[:, :, :nv], xa[:, :, :nv], xb[:, :, nv:], xa[:, :, nv:], 0)
    visc_rad, up_f, dn_f = viscous(state, weight, rb[:, :, :nv], ra[:, :, :nv], rb[:, :, nv:], ra[:, :, nv:], 1)
    spread = 0.5 * (up_f - dn_f)
    mixed = jac_radial[0][None, None, :, None] * spread[:, :, 0:1]
    for k in range(1, nv):
        mixed = mixed + jac_radial[k][None, None, :, None] * spread[:, :, k:k + 1]
    return viscosity * visc_ax + (mixed + viscosity * visc_rad)


def line_kernel(jac_ref, lines_ref, mats_ref, out_ref):
    S, V, XL, C = lines_ref.shape
    nx = S * XL
    cols = [lines_ref[:, v, :, :].reshape(nx, C) for v in range(V)]
    wide = jnp.concatenate(cols, axis=1)
    prod = jnp.dot(
        mats_ref[...], wide, precision=lax.Precision.HIGHEST, preferred_element_type=jnp.float32
    )
    smooth = prod[:nx]
    slope = prod[nx:]
    for v in range(V):
        mix = jac_ref[0, v] * slope[:, 0:C]
        for k in range(1, V):
            mix = mix + jac_ref[k, v] * slope[:, k * C:(k + 1) * C]
        res = cols[v] - smooth[:, v * C:(v + 1) * C] + section_step * mix
        out_ref[:, v, :, :] = res.reshape(S, XL, C)


def line_section(lines, mats, jac_axial):
    S, V, XL, C = lines.shape
    return pl.pallas_call(
        line_kernel,
        out_shape=jax.ShapeDtypeStruct(lines.shape, lines.dtype),
        in_specs=[
            pl.BlockSpec(memory_space=pltpu.SMEM),
            pl.BlockSpec(memory_space=pltpu.VMEM),
            pl.BlockSpec(memory_space=pltpu.VMEM),
        ],
        out_specs=pl.BlockSpec(memory_space=pltpu.VMEM),
        compiler_params=pltpu.CompilerParams(vmem_limit_bytes=48 * 1024 * 1024),
    )(jac_axial, lines, mats)


def body(state, metric, deriv, filt_corr, jac_axial, jac_radial):
    nx, nr, nv, na = state.shape
    peers = lax.axis_size("ax")
    assert nr == peers
    mats = jnp.concatenate([filt_corr, deriv], axis=0)
    weight = metric.reshape(metric.shape[0], metric.shape[1], 1, metric.shape[2])
    packed = jnp.concatenate([state, weight], axis=2)
    ax_halo = halos(packed, "ax", 0)
    rad_halo = halos(packed, "rad", 1)
    send = jnp.transpose(state, (1, 2, 0, 3))
    send, ax_halo, rad_halo = lax.optimization_barrier((send, ax_halo, rad_halo))
    lines = lax.all_to_all(send, "ax", split_axis=0, concat_axis=0, tiled=True)
    local = stencil(state, weight, ax_halo, rad_halo, jac_radial)
    lines, local = lax.optimization_barrier((lines, local))
    res = line_section(lines, mats, jac_axial)
    ret = lax.all_to_all(res, "ax", split_axis=0, concat_axis=0, tiled=True)
    return jnp.transpose(ret, (2, 0, 1, 3)) + section_step * local


def solution(mesh):
    in_specs = (P("ax", "rad", None, None), P("ax", "rad", None), P(), P(), P(), P())
    out_specs = P("ax", "rad", None, None)
    return jax.shard_map(body, mesh=mesh, in_specs=in_specs, out_specs=out_specs, check_vma=False)
```

```python
import functools

import jax
import jax.numpy as jnp
from jax import lax
from jax.experimental import pallas as pl
from jax.experimental.pallas import tpu as pltpu
from jax.sharding import PartitionSpec as P

section_step = 0.25
viscosity = 0.5


def halos(x, axis, dim):
    peers, length = (lax.axis_size(axis), x.shape[dim])
    up = [(i, (i + 1) % peers) for i in range(peers - 1)]
    down = [(j, i) for i, j in up]
    last = lax.slice_in_dim(x, length - 1, length, axis=dim)
    leading = lax.slice_in_dim(x, 0, 1, axis=dim)
    return lax.ppermute(last, axis, up), lax.ppermute(leading, axis, down)


def viscous(field, weight, before, after, wbefore, wafter, dim):
    up_f = jnp.concatenate([lax.slice_in_dim(field, 1, field.shape[dim], axis=dim), after], axis=dim)
    dn_f = jnp.concatenate([before, lax.slice_in_dim(field, 0, field.shape[dim] - 1, axis=dim)], axis=dim)
    up_w = jnp.concatenate([lax.slice_in_dim(weight, 1, weight.shape[dim], axis=dim), wafter], axis=dim)
    dn_w = jnp.concatenate([wbefore, lax.slice_in_dim(weight, 0, weight.shape[dim] - 1, axis=dim)], axis=dim)
    upper = 0.5 * (weight + up_w)
    lower = 0.5 * (weight + dn_w)
    return upper * (up_f - field) - lower * (field - dn_f), up_f, dn_f


def stencil(state, weight, ax_halo, rad_halo, jac_radial):
    nv = state.shape[2]
    (xb, xa), (rb, ra) = ax_halo, rad_halo
    visc_ax, _, _ = viscous(state, weight, xb[:, :, :nv], xa[:, :, :nv], xb[:, :, nv:], xa[:, :, nv:], 0)
    visc_rad, up_f, dn_f = viscous(state, weight, rb[:, :, :nv], ra[:, :, :nv], rb[:, :, nv:], ra[:, :, nv:], 1)
    spread = 0.5 * (up_f - dn_f)
    mixed = jac_radial[0][None, None, :, None] * spread[:, :, 0:1]
    for k in range(1, nv):
        mixed = mixed + jac_radial[k][None, None, :, None] * spread[:, :, k:k + 1]
    return viscosity * visc_ax + (mixed + viscosity * visc_rad)


def line_kernel(jac_ref, lines_ref, mats_ref, out_ref):
    S, V, XL, C = lines_ref.shape
    nx = S * XL
    cols = [lines_ref[:, v, :, :].reshape(nx, C) for v in range(V)]
    wide = jnp.concatenate(cols, axis=1)
    prod = jnp.dot(
        mats_ref[...], wide, precision=lax.Precision.HIGHEST, preferred_element_type=jnp.float32
    )
    smooth = prod[:nx]
    slope = prod[nx:]
    for v in range(V):
        mix = jac_ref[0, v] * slope[:, 0:C]
        for k in range(1, V):
            mix = mix + jac_ref[k, v] * slope[:, k * C:(k + 1) * C]
        res = cols[v] - smooth[:, v * C:(v + 1) * C] + section_step * mix
        out_ref[:, v, :, :] = res.reshape(S, XL, C)


def line_section(lines, mats, jac_axial):
    S, V, XL, C = lines.shape
    return pl.pallas_call(
        line_kernel,
        out_shape=jax.ShapeDtypeStruct(lines.shape, lines.dtype),
        in_specs=[
            pl.BlockSpec(memory_space=pltpu.SMEM),
            pl.BlockSpec(memory_space=pltpu.VMEM),
            pl.BlockSpec(memory_space=pltpu.VMEM),
        ],
        out_specs=pl.BlockSpec(memory_space=pltpu.VMEM),
        compiler_params=pltpu.CompilerParams(vmem_limit_bytes=48 * 1024 * 1024),
    )(jac_axial, lines, mats)


def body(state, metric, deriv, filt_corr, jac_axial, jac_radial):
    nx, nr, nv, na = state.shape
    peers = lax.axis_size("ax")
    assert nr == peers
    mats = jnp.concatenate([filt_corr, deriv], axis=0)
    weight = metric.reshape(metric.shape[0], metric.shape[1], 1, metric.shape[2])
    packed = jnp.concatenate([state, weight], axis=2)
    send = jnp.transpose(state, (1, 2, 0, 3))
    lines = lax.all_to_all(send, "ax", split_axis=0, concat_axis=0, tiled=True)
    lines, packed = lax.optimization_barrier((lines, packed))
    ax_halo = halos(packed, "ax", 0)
    rad_halo = halos(packed, "rad", 1)
    res = line_section(lines, mats, jac_axial)
    res, ax_halo, rad_halo = lax.optimization_barrier((res, ax_halo, rad_halo))
    ret = lax.all_to_all(res, "ax", split_axis=0, concat_axis=0, tiled=True)
    local = stencil(state, weight, ax_halo, rad_halo, jac_radial)
    ret, local = lax.optimization_barrier((ret, local))
    return jnp.transpose(ret, (2, 0, 1, 3)) + section_step * local


def solution(mesh):
    in_specs = (P("ax", "rad", None, None), P("ax", "rad", None), P(), P(), P(), P())
    out_specs = P("ax", "rad", None, None)
    return jax.shard_map(body, mesh=mesh, in_specs=in_specs, out_specs=out_specs, check_vma=False)
```

```python
import functools

import jax
import jax.numpy as jnp
from jax import lax
from jax.experimental import pallas as pl
from jax.experimental.pallas import tpu as pltpu
from jax.sharding import PartitionSpec as P

section_step = 0.25
viscosity = 0.5


def halos(x, axis, dim):
    peers, length = (lax.axis_size(axis), x.shape[dim])
    up = [(i, (i + 1) % peers) for i in range(peers - 1)]
    down = [(j, i) for i, j in up]
    last = lax.slice_in_dim(x, length - 1, length, axis=dim)
    leading = lax.slice_in_dim(x, 0, 1, axis=dim)
    return lax.ppermute(last, axis, up), lax.ppermute(leading, axis, down)


def viscous(field, weight, before, after, wbefore, wafter, dim):
    up_f = jnp.concatenate([lax.slice_in_dim(field, 1, field.shape[dim], axis=dim), after], axis=dim)
    dn_f = jnp.concatenate([before, lax.slice_in_dim(field, 0, field.shape[dim] - 1, axis=dim)], axis=dim)
    up_w = jnp.concatenate([lax.slice_in_dim(weight, 1, weight.shape[dim], axis=dim), wafter], axis=dim)
    dn_w = jnp.concatenate([wbefore, lax.slice_in_dim(weight, 0, weight.shape[dim] - 1, axis=dim)], axis=dim)
    upper = 0.5 * (weight + up_w)
    lower = 0.5 * (weight + dn_w)
    return upper * (up_f - field) - lower * (field - dn_f), up_f, dn_f


def stencil(state, weight, ax_halo, rad_halo, jac_radial):
    nv = state.shape[2]
    (xb, xa), (rb, ra) = ax_halo, rad_halo
    visc_ax, _, _ = viscous(state, weight, xb[:, :, :nv], xa[:, :, :nv], xb[:, :, nv:], xa[:, :, nv:], 0)
    visc_rad, up_f, dn_f = viscous(state, weight, rb[:, :, :nv], ra[:, :, :nv], rb[:, :, nv:], ra[:, :, nv:], 1)
    spread = 0.5 * (up_f - dn_f)
    mixed = jac_radial[0][None, None, :, None] * spread[:, :, 0:1]
    for k in range(1, nv):
        mixed = mixed + jac_radial[k][None, None, :, None] * spread[:, :, k:k + 1]
    return viscosity * visc_ax + (mixed + viscosity * visc_rad)


def line_kernel(jac_ref, lines_ref, mats_ref, out_ref):
    S, V, XL, C = lines_ref.shape
    nx = S * XL
    cols = [lines_ref[:, v, :, :].reshape(nx, C) for v in range(V)]
    wide = jnp.concatenate(cols, axis=1)
    prod = jnp.dot(
        mats_ref[...], wide, precision=lax.Precision.HIGHEST, preferred_element_type=jnp.float32
    )
    smooth = prod[:nx]
    slope = prod[nx:]
    for v in range(V):
        mix = jac_ref[0, v] * slope[:, 0:C]
        for k in range(1, V):
            mix = mix + jac_ref[k, v] * slope[:, k * C:(k + 1) * C]
        res = cols[v] - smooth[:, v * C:(v + 1) * C] + section_step * mix
        out_ref[:, v, :, :] = res.reshape(S, XL, C)


def line_section(lines, mats, jac_axial):
    S, V, XL, C = lines.shape
    return pl.pallas_call(
        line_kernel,
        out_shape=jax.ShapeDtypeStruct(lines.shape, lines.dtype),
        in_specs=[
            pl.BlockSpec(memory_space=pltpu.SMEM),
            pl.BlockSpec(memory_space=pltpu.VMEM),
            pl.BlockSpec(memory_space=pltpu.VMEM),
        ],
        out_specs=pl.BlockSpec(memory_space=pltpu.VMEM),
        compiler_params=pltpu.CompilerParams(vmem_limit_bytes=48 * 1024 * 1024),
    )(jac_axial, lines, mats)


def body(state, metric, deriv, filt_corr, jac_axial, jac_radial):
    nx, nr, nv, na = state.shape
    peers = lax.axis_size("ax")
    assert nr == peers
    mats = jnp.concatenate([filt_corr, deriv], axis=0)
    weight = metric.reshape(metric.shape[0], metric.shape[1], 1, metric.shape[2])
    packed = jnp.concatenate([state, weight], axis=2)
    send = jnp.transpose(state, (1, 2, 0, 3))
    lines = lax.all_to_all(send, "ax", split_axis=0, concat_axis=0, tiled=True)
    ax_halo = halos(packed, "ax", 0)
    rad_halo = halos(packed, "rad", 1)
    res = line_section(lines, mats, jac_axial)
    res, ax_halo, rad_halo = lax.optimization_barrier((res, ax_halo, rad_halo))
    ret = lax.all_to_all(res, "ax", split_axis=0, concat_axis=0, tiled=True)
    local = stencil(state, weight, ax_halo, rad_halo, jac_radial)
    ret, local = lax.optimization_barrier((ret, local))
    return jnp.transpose(ret, (2, 0, 1, 3)) + section_step * local


def solution(mesh):
    in_specs = (P("ax", "rad", None, None), P("ax", "rad", None), P(), P(), P(), P())
    out_specs = P("ax", "rad", None, None)
    return jax.shard_map(body, mesh=mesh, in_specs=in_specs, out_specs=out_specs, check_vma=False)
```

```python
import functools

import jax
import jax.numpy as jnp
from jax import lax
from jax.experimental import pallas as pl
from jax.experimental.pallas import tpu as pltpu
from jax.sharding import PartitionSpec as P

section_step = 0.25
viscosity = 0.5


def halos(x, axis, dim):
    peers, length = (lax.axis_size(axis), x.shape[dim])
    up = [(i, (i + 1) % peers) for i in range(peers - 1)]
    down = [(j, i) for i, j in up]
    last = lax.slice_in_dim(x, length - 1, length, axis=dim)
    leading = lax.slice_in_dim(x, 0, 1, axis=dim)
    return lax.ppermute(last, axis, up), lax.ppermute(leading, axis, down)


def viscous(field, weight, before, after, wbefore, wafter, dim):
    up_f = jnp.concatenate([lax.slice_in_dim(field, 1, field.shape[dim], axis=dim), after], axis=dim)
    dn_f = jnp.concatenate([before, lax.slice_in_dim(field, 0, field.shape[dim] - 1, axis=dim)], axis=dim)
    up_w = jnp.concatenate([lax.slice_in_dim(weight, 1, weight.shape[dim], axis=dim), wafter], axis=dim)
    dn_w = jnp.concatenate([wbefore, lax.slice_in_dim(weight, 0, weight.shape[dim] - 1, axis=dim)], axis=dim)
    upper = 0.5 * (weight + up_w)
    lower = 0.5 * (weight + dn_w)
    return upper * (up_f - field) - lower * (field - dn_f), up_f, dn_f


def stencil(state, weight, ax_halo, rad_halo, jac_radial):
    nv = state.shape[2]
    (xb, xa), (rb, ra) = ax_halo, rad_halo
    visc_ax, _, _ = viscous(state, weight, xb[:, :, :nv], xa[:, :, :nv], xb[:, :, nv:], xa[:, :, nv:], 0)
    visc_rad, up_f, dn_f = viscous(state, weight, rb[:, :, :nv], ra[:, :, :nv], rb[:, :, nv:], ra[:, :, nv:], 1)
    spread = 0.5 * (up_f - dn_f)
    mixed = jac_radial[0][None, None, :, None] * spread[:, :, 0:1]
    for k in range(1, nv):
        mixed = mixed + jac_radial[k][None, None, :, None] * spread[:, :, k:k + 1]
    return viscosity * visc_ax + (mixed + viscosity * visc_rad)


def split_bf16(x):
    t = x * 65537.0
    hi = t - (t - x)
    return hi.astype(jnp.bfloat16), (x - hi).astype(jnp.bfloat16)


def line_kernel(jac_ref, lines_ref, mats_ref, out_ref):
    S, V, XL, C = lines_ref.shape
    nx = S * XL
    cols = [lines_ref[:, v, :, :].reshape(nx, C) for v in range(V)]
    wide = jnp.concatenate(cols, axis=1)
    w_hi, w_lo = split_bf16(wide)
    m_hi, m_lo = split_bf16(mats_ref[...])
    prod = jnp.dot(m_hi, w_hi, preferred_element_type=jnp.float32)
    prod = prod + jnp.dot(m_hi, w_lo, preferred_element_type=jnp.float32)
    prod = prod + jnp.dot(m_lo, w_hi, preferred_element_type=jnp.float32)
    smooth = prod[:nx]
    slope = prod[nx:]
    for v in range(V):
        mix = jac_ref[0, v] * slope[:, 0:C]
        for k in range(1, V):
            mix = mix + jac_ref[k, v] * slope[:, k * C:(k + 1) * C]
        res = cols[v] - smooth[:, v * C:(v + 1) * C] + section_step * mix
        out_ref[:, v, :, :] = res.reshape(S, XL, C)


def line_section(lines, mats, jac_axial):
    S, V, XL, A = lines.shape
    C = 128 if A % 128 == 0 else A
    block = pl.BlockSpec((S, V, XL, C), lambda i: (0, 0, 0, i))
    whole = pl.BlockSpec(mats.shape, lambda i: (0, 0))
    return pl.pallas_call(
        line_kernel,
        out_shape=jax.ShapeDtypeStruct(lines.shape, lines.dtype),
        grid=(A // C,),
        in_specs=[pl.BlockSpec(memory_space=pltpu.SMEM), block, whole],
        out_specs=block,
        compiler_params=pltpu.CompilerParams(vmem_limit_bytes=48 * 1024 * 1024),
    )(jac_axial, lines, mats)


def body(state, metric, deriv, filt_corr, jac_axial, jac_radial):
    nx, nr, nv, na = state.shape
    peers = lax.axis_size("ax")
    assert nr == peers
    mats = jnp.concatenate([filt_corr, deriv], axis=0)
    weight = metric.reshape(metric.shape[0], metric.shape[1], 1, metric.shape[2])
    packed = jnp.concatenate([state, weight], axis=2)
    send = jnp.transpose(state, (1, 2, 0, 3))
    lines = lax.all_to_all(send, "ax", split_axis=0, concat_axis=0, tiled=True)
    ax_halo = halos(packed, "ax", 0)
    rad_halo = halos(packed, "rad", 1)
    res = line_section(lines, mats, jac_axial)
    res, ax_halo, rad_halo = lax.optimization_barrier((res, ax_halo, rad_halo))
    ret = lax.all_to_all(res, "ax", split_axis=0, concat_axis=0, tiled=True)
    local = stencil(state, weight, ax_halo, rad_halo, jac_radial)
    ret, local = lax.optimization_barrier((ret, local))
    return jnp.transpose(ret, (2, 0, 1, 3)) + section_step * local


def solution(mesh):
    in_specs = (P("ax", "rad", None, None), P("ax", "rad", None), P(), P(), P(), P())
    out_specs = P("ax", "rad", None, None)
    return jax.shard_map(body, mesh=mesh, in_specs=in_specs, out_specs=out_specs, check_vma=False)
```

```python
import functools

import jax
import jax.numpy as jnp
from jax import lax
from jax.experimental import pallas as pl
from jax.experimental.pallas import tpu as pltpu
from jax.experimental.layout import Layout, with_layout_constraint
from jax.sharding import PartitionSpec as P

section_step = 0.25
viscosity = 0.5


def halos(x, axis, dim):
    peers, length = (lax.axis_size(axis), x.shape[dim])
    up = [(i, (i + 1) % peers) for i in range(peers - 1)]
    down = [(j, i) for i, j in up]
    last = lax.slice_in_dim(x, length - 1, length, axis=dim)
    leading = lax.slice_in_dim(x, 0, 1, axis=dim)
    return lax.ppermute(last, axis, up), lax.ppermute(leading, axis, down)


def viscous(field, weight, before, after, wbefore, wafter, dim):
    up_f = jnp.concatenate([lax.slice_in_dim(field, 1, field.shape[dim], axis=dim), after], axis=dim)
    dn_f = jnp.concatenate([before, lax.slice_in_dim(field, 0, field.shape[dim] - 1, axis=dim)], axis=dim)
    up_w = jnp.concatenate([lax.slice_in_dim(weight, 1, weight.shape[dim], axis=dim), wafter], axis=dim)
    dn_w = jnp.concatenate([wbefore, lax.slice_in_dim(weight, 0, weight.shape[dim] - 1, axis=dim)], axis=dim)
    upper = 0.5 * (weight + up_w)
    lower = 0.5 * (weight + dn_w)
    return upper * (up_f - field) - lower * (field - dn_f), up_f, dn_f


def stencil(state, weight, ax_halo, rad_halo, jac_radial):
    nv = state.shape[2]
    (xb, xa), (rb, ra) = ax_halo, rad_halo
    visc_ax, _, _ = viscous(state, weight, xb[:, :, :nv], xa[:, :, :nv], xb[:, :, nv:], xa[:, :, nv:], 0)
    visc_rad, up_f, dn_f = viscous(state, weight, rb[:, :, :nv], ra[:, :, :nv], rb[:, :, nv:], ra[:, :, nv:], 1)
    spread = 0.5 * (up_f - dn_f)
    mixed = jac_radial[0][None, None, :, None] * spread[:, :, 0:1]
    for k in range(1, nv):
        mixed = mixed + jac_radial[k][None, None, :, None] * spread[:, :, k:k + 1]
    return viscosity * visc_ax + (mixed + viscosity * visc_rad)


def split_bf16(x):
    t = x * 65537.0
    hi = t - (t - x)
    return hi.astype(jnp.bfloat16), (x - hi).astype(jnp.bfloat16)


def line_kernel(jac_ref, lines_ref, mats_ref, out_ref):
    S, V, XL, C = lines_ref.shape
    nx = S * XL
    cols = [lines_ref[:, v, :, :].reshape(nx, C) for v in range(V)]
    wide = jnp.concatenate(cols, axis=1)
    w_hi, w_lo = split_bf16(wide)
    m_hi, m_lo = split_bf16(mats_ref[...])
    prod = jnp.dot(m_hi, w_hi, preferred_element_type=jnp.float32)
    prod = prod + jnp.dot(m_hi, w_lo, preferred_element_type=jnp.float32)
    prod = prod + jnp.dot(m_lo, w_hi, preferred_element_type=jnp.float32)
    smooth = prod[:nx]
    slope = prod[nx:]
    for v in range(V):
        mix = jac_ref[0, v] * slope[:, 0:C]
        for k in range(1, V):
            mix = mix + jac_ref[k, v] * slope[:, k * C:(k + 1) * C]
        res = cols[v] - smooth[:, v * C:(v + 1) * C] + section_step * mix
        out_ref[:, v, :, :] = res.reshape(S, XL, C)


def line_section(lines, mats, jac_axial):
    S, V, XL, A = lines.shape
    C = 128 if A % 128 == 0 else A
    block = pl.BlockSpec((S, V, XL, C), lambda i: (0, 0, 0, i))
    whole = pl.BlockSpec(mats.shape, lambda i: (0, 0))
    return pl.pallas_call(
        line_kernel,
        out_shape=jax.ShapeDtypeStruct(lines.shape, lines.dtype),
        grid=(A // C,),
        in_specs=[pl.BlockSpec(memory_space=pltpu.SMEM), block, whole],
        out_specs=block,
        compiler_params=pltpu.CompilerParams(vmem_limit_bytes=48 * 1024 * 1024),
    )(jac_axial, lines, mats)


def body(state, metric, deriv, filt_corr, jac_axial, jac_radial):
    nx, nr, nv, na = state.shape
    peers = lax.axis_size("ax")
    assert nr == peers
    mats = jnp.concatenate([filt_corr, deriv], axis=0)
    weight = metric.reshape(metric.shape[0], metric.shape[1], 1, metric.shape[2])
    packed = jnp.concatenate([state, weight], axis=2)
    send = jnp.transpose(state, (1, 2, 0, 3))
    lines = lax.all_to_all(send, "ax", split_axis=0, concat_axis=0, tiled=True)
    ax_halo = halos(packed, "ax", 0)
    rad_halo = halos(packed, "rad", 1)
    res = line_section(lines, mats, jac_axial)
    res, ax_halo, rad_halo = lax.optimization_barrier((res, ax_halo, rad_halo))
    ret = lax.all_to_all(res, "ax", split_axis=0, concat_axis=0, tiled=True)
    local = stencil(state, weight, ax_halo, rad_halo, jac_radial)
    local = with_layout_constraint(local, Layout(major_to_minor=(0, 2, 1, 3)))
    ret, local = lax.optimization_barrier((ret, local))
    return jnp.transpose(ret, (2, 0, 1, 3)) + section_step * local


def solution(mesh):
    in_specs = (P("ax", "rad", None, None), P("ax", "rad", None), P(), P(), P(), P())
    out_specs = P("ax", "rad", None, None)
    return jax.shard_map(body, mesh=mesh, in_specs=in_specs, out_specs=out_specs, check_vma=False)
```

```python
import functools

import jax
import jax.numpy as jnp
from jax import lax
from jax.experimental import pallas as pl
from jax.experimental.pallas import tpu as pltpu
from jax.experimental.layout import Layout, with_layout_constraint
from jax.sharding import PartitionSpec as P

section_step = 0.25
viscosity = 0.5


def halos(x, axis, dim):
    peers, length = (lax.axis_size(axis), x.shape[dim])
    up = [(i, (i + 1) % peers) for i in range(peers - 1)]
    down = [(j, i) for i, j in up]
    last = lax.slice_in_dim(x, length - 1, length, axis=dim)
    leading = lax.slice_in_dim(x, 0, 1, axis=dim)
    return lax.ppermute(last, axis, up), lax.ppermute(leading, axis, down)


def viscous(field, weight, before, after, wbefore, wafter, dim):
    up_f = jnp.concatenate([lax.slice_in_dim(field, 1, field.shape[dim], axis=dim), after], axis=dim)
    dn_f = jnp.concatenate([before, lax.slice_in_dim(field, 0, field.shape[dim] - 1, axis=dim)], axis=dim)
    up_w = jnp.concatenate([lax.slice_in_dim(weight, 1, weight.shape[dim], axis=dim), wafter], axis=dim)
    dn_w = jnp.concatenate([wbefore, lax.slice_in_dim(weight, 0, weight.shape[dim] - 1, axis=dim)], axis=dim)
    upper = 0.5 * (weight + up_w)
    lower = 0.5 * (weight + dn_w)
    return upper * (up_f - field) - lower * (field - dn_f), up_f, dn_f


def stencil(state, weight, ax_halo, rad_halo, jac_radial):
    nv = state.shape[2]
    (xb, xa), (rb, ra) = ax_halo, rad_halo
    visc_ax, _, _ = viscous(state, weight, xb[:, :, :nv], xa[:, :, :nv], xb[:, :, nv:], xa[:, :, nv:], 0)
    visc_rad, up_f, dn_f = viscous(state, weight, rb[:, :, :nv], ra[:, :, :nv], rb[:, :, nv:], ra[:, :, nv:], 1)
    spread = 0.5 * (up_f - dn_f)
    mixed = jac_radial[0][None, None, :, None] * spread[:, :, 0:1]
    for k in range(1, nv):
        mixed = mixed + jac_radial[k][None, None, :, None] * spread[:, :, k:k + 1]
    return viscosity * visc_ax + (mixed + viscosity * visc_rad)


def split_bf16(x):
    t = x * 65537.0
    hi = t - (t - x)
    return hi.astype(jnp.bfloat16), (x - hi).astype(jnp.bfloat16)


def line_kernel(jac_ref, lines_ref, mats_ref, out_ref):
    S, V, XL, C = lines_ref.shape
    nx = S * XL
    cols = [lines_ref[:, v, :, :].reshape(nx, C) for v in range(V)]
    wide = jnp.concatenate(cols, axis=1)
    w_hi, w_lo = split_bf16(wide)
    m_hi, m_lo = split_bf16(mats_ref[...])
    prod = jnp.dot(m_hi, w_hi, preferred_element_type=jnp.float32)
    prod = prod + jnp.dot(m_hi, w_lo, preferred_element_type=jnp.float32)
    prod = prod + jnp.dot(m_lo, w_hi, preferred_element_type=jnp.float32)
    smooth = prod[:nx]
    slope = prod[nx:]
    for v in range(V):
        mix = jac_ref[0, v] * slope[:, 0:C]
        for k in range(1, V):
            mix = mix + jac_ref[k, v] * slope[:, k * C:(k + 1) * C]
        res = cols[v] - smooth[:, v * C:(v + 1) * C] + section_step * mix
        out_ref[:, v, :, :] = res.reshape(S, XL, C)


def line_section(lines, mats, jac_axial):
    S, V, XL, A = lines.shape
    C = 128 if A % 128 == 0 else A
    block = pl.BlockSpec((S, V, XL, C), lambda i: (0, 0, 0, i))
    whole = pl.BlockSpec(mats.shape, lambda i: (0, 0))
    return pl.pallas_call(
        line_kernel,
        out_shape=jax.ShapeDtypeStruct(lines.shape, lines.dtype),
        grid=(A // C,),
        in_specs=[pl.BlockSpec(memory_space=pltpu.SMEM), block, whole],
        out_specs=block,
        compiler_params=pltpu.CompilerParams(vmem_limit_bytes=48 * 1024 * 1024),
    )(jac_axial, lines, mats)


def body(state, metric, deriv, filt_corr, jac_axial, jac_radial):
    nx, nr, nv, na = state.shape
    peers = lax.axis_size("ax")
    assert nr == peers
    mats = jnp.concatenate([filt_corr, deriv], axis=0)
    weight = metric.reshape(metric.shape[0], metric.shape[1], 1, metric.shape[2])
    packed = jnp.concatenate([state, weight], axis=2)
    send = jnp.transpose(state, (1, 2, 0, 3))
    lines = lax.all_to_all(send, "ax", split_axis=0, concat_axis=0, tiled=True)
    ax_halo = halos(packed, "ax", 0)
    rad_halo = halos(packed, "rad", 1)
    cut = (na // 3 // 128) * 256 if na % 384 == 0 else na
    first = line_section(lines[..., :cut], mats, jac_axial)
    first, ax_halo, rad_halo = lax.optimization_barrier((first, ax_halo, rad_halo))
    rets = [lax.all_to_all(first, "ax", split_axis=0, concat_axis=0, tiled=True)]
    if cut < na:
        second = line_section(lines[..., cut:], mats, jac_axial)
        rets[0], second = lax.optimization_barrier((rets[0], second))
        rets.append(lax.all_to_all(second, "ax", split_axis=0, concat_axis=0, tiled=True))
    local = stencil(state, weight, ax_halo, rad_halo, jac_radial)
    local = with_layout_constraint(local, Layout(major_to_minor=(0, 2, 1, 3)))
    rets, local = lax.optimization_barrier((rets, local))
    bounds = [0, cut, na][:len(rets) + 1]
    parts = [
        jnp.transpose(r, (2, 0, 1, 3)) + section_step * local[..., lo:hi]
        for r, lo, hi in zip(rets, bounds[:-1], bounds[1:])
    ]
    return jnp.concatenate(parts, axis=3)


def solution(mesh):
    in_specs = (P("ax", "rad", None, None), P("ax", "rad", None), P(), P(), P(), P())
    out_specs = P("ax", "rad", None, None)
    return jax.shard_map(body, mesh=mesh, in_specs=in_specs, out_specs=out_specs, check_vma=False)
```

```python
import functools

import jax
import jax.numpy as jnp
from jax import lax
from jax.experimental import pallas as pl
from jax.experimental.pallas import tpu as pltpu
from jax.experimental.layout import Layout, with_layout_constraint
from jax.sharding import PartitionSpec as P

section_step = 0.25
viscosity = 0.5


def halos(x, axis, dim):
    peers, length = (lax.axis_size(axis), x.shape[dim])
    up = [(i, (i + 1) % peers) for i in range(peers - 1)]
    down = [(j, i) for i, j in up]
    last = lax.slice_in_dim(x, length - 1, length, axis=dim)
    leading = lax.slice_in_dim(x, 0, 1, axis=dim)
    return lax.ppermute(last, axis, up), lax.ppermute(leading, axis, down)


def viscous(field, weight, before, after, wbefore, wafter, dim):
    up_f = jnp.concatenate([lax.slice_in_dim(field, 1, field.shape[dim], axis=dim), after], axis=dim)
    dn_f = jnp.concatenate([before, lax.slice_in_dim(field, 0, field.shape[dim] - 1, axis=dim)], axis=dim)
    up_w = jnp.concatenate([lax.slice_in_dim(weight, 1, weight.shape[dim], axis=dim), wafter], axis=dim)
    dn_w = jnp.concatenate([wbefore, lax.slice_in_dim(weight, 0, weight.shape[dim] - 1, axis=dim)], axis=dim)
    upper = 0.5 * (weight + up_w)
    lower = 0.5 * (weight + dn_w)
    return upper * (up_f - field) - lower * (field - dn_f), up_f, dn_f


def stencil(state, weight, ax_halo, rad_halo, jac_radial):
    nv = state.shape[2]
    (xb, xa), (rb, ra) = ax_halo, rad_halo
    visc_ax, _, _ = viscous(state, weight, xb[:, :, :nv], xa[:, :, :nv], xb[:, :, nv:], xa[:, :, nv:], 0)
    visc_rad, up_f, dn_f = viscous(state, weight, rb[:, :, :nv], ra[:, :, :nv], rb[:, :, nv:], ra[:, :, nv:], 1)
    spread = 0.5 * (up_f - dn_f)
    mixed = jac_radial[0][None, None, :, None] * spread[:, :, 0:1]
    for k in range(1, nv):
        mixed = mixed + jac_radial[k][None, None, :, None] * spread[:, :, k:k + 1]
    return viscosity * visc_ax + (mixed + viscosity * visc_rad)


def split_bf16(x):
    t = x * 65537.0
    hi = t - (t - x)
    return hi.astype(jnp.bfloat16), (x - hi).astype(jnp.bfloat16)


def line_kernel(jac_ref, lines_ref, mats_ref, out_ref):
    S, V, XL, C = lines_ref.shape
    nx = S * XL
    cols = [lines_ref[:, v, :, :].reshape(nx, C) for v in range(V)]
    wide = jnp.concatenate(cols, axis=1)
    w_hi, w_lo = split_bf16(wide)
    m_hi, m_lo = split_bf16(mats_ref[...])
    prod = jnp.dot(m_hi, w_hi, preferred_element_type=jnp.float32)
    prod = prod + jnp.dot(m_hi, w_lo, preferred_element_type=jnp.float32)
    prod = prod + jnp.dot(m_lo, w_hi, preferred_element_type=jnp.float32)
    smooth = prod[:nx]
    slope = prod[nx:]
    for v in range(V):
        mix = jac_ref[0, v] * slope[:, 0:C]
        for k in range(1, V):
            mix = mix + jac_ref[k, v] * slope[:, k * C:(k + 1) * C]
        res = cols[v] - smooth[:, v * C:(v + 1) * C] + section_step * mix
        out_ref[:, v, :, :] = res.reshape(S, XL, C)


def line_section(lines, mats, jac_axial):
    S, V, XL, A = lines.shape
    C = 128 if A % 128 == 0 else A
    block = pl.BlockSpec((S, V, XL, C), lambda i: (0, 0, 0, i))
    whole = pl.BlockSpec(mats.shape, lambda i: (0, 0))
    return pl.pallas_call(
        line_kernel,
        out_shape=jax.ShapeDtypeStruct(lines.shape, lines.dtype),
        grid=(A // C,),
        in_specs=[pl.BlockSpec(memory_space=pltpu.SMEM), block, whole],
        out_specs=block,
        input_output_aliases={1: 0},
        compiler_params=pltpu.CompilerParams(vmem_limit_bytes=48 * 1024 * 1024),
    )(jac_axial, lines, mats)


def body(state, metric, deriv, filt_corr, jac_axial, jac_radial):
    nx, nr, nv, na = state.shape
    peers = lax.axis_size("ax")
    assert nr == peers
    mats = jnp.concatenate([filt_corr, deriv], axis=0)
    weight = metric.reshape(metric.shape[0], metric.shape[1], 1, metric.shape[2])
    packed = jnp.concatenate([state, weight], axis=2)
    send = jnp.transpose(state, (1, 2, 0, 3))
    lines = lax.all_to_all(send, "ax", split_axis=0, concat_axis=0, tiled=True)
    ax_halo = halos(packed, "ax", 0)
    rad_halo = halos(packed, "rad", 1)
    res = line_section(lines, mats, jac_axial)
    res, ax_halo, rad_halo = lax.optimization_barrier((res, ax_halo, rad_halo))
    ret = lax.all_to_all(res, "ax", split_axis=0, concat_axis=0, tiled=True)
    local = stencil(state, weight, ax_halo, rad_halo, jac_radial)
    local = with_layout_constraint(local, Layout(major_to_minor=(0, 2, 1, 3)))
    ret, local = lax.optimization_barrier((ret, local))
    return jnp.transpose(ret, (2, 0, 1, 3)) + section_step * local


def solution(mesh):
    in_specs = (P("ax", "rad", None, None), P("ax", "rad", None), P(), P(), P(), P())
    out_specs = P("ax", "rad", None, None)
    return jax.shard_map(body, mesh=mesh, in_specs=in_specs, out_specs=out_specs, check_vma=False)
```

```python
import functools

import jax
import jax.numpy as jnp
from jax import lax
from jax.experimental import pallas as pl
from jax.experimental.pallas import tpu as pltpu
from jax.experimental.layout import Layout, with_layout_constraint
from jax.sharding import PartitionSpec as P

section_step = 0.25
viscosity = 0.5


def halos(x, axis, dim):
    peers, length = (lax.axis_size(axis), x.shape[dim])
    up = [(i, (i + 1) % peers) for i in range(peers - 1)]
    down = [(j, i) for i, j in up]
    last = lax.slice_in_dim(x, length - 1, length, axis=dim)
    leading = lax.slice_in_dim(x, 0, 1, axis=dim)
    return lax.ppermute(last, axis, up), lax.ppermute(leading, axis, down)


def viscous(field, weight, before, after, wbefore, wafter, dim):
    up_f = jnp.concatenate([lax.slice_in_dim(field, 1, field.shape[dim], axis=dim), after], axis=dim)
    dn_f = jnp.concatenate([before, lax.slice_in_dim(field, 0, field.shape[dim] - 1, axis=dim)], axis=dim)
    up_w = jnp.concatenate([lax.slice_in_dim(weight, 1, weight.shape[dim], axis=dim), wafter], axis=dim)
    dn_w = jnp.concatenate([wbefore, lax.slice_in_dim(weight, 0, weight.shape[dim] - 1, axis=dim)], axis=dim)
    upper = 0.5 * (weight + up_w)
    lower = 0.5 * (weight + dn_w)
    return upper * (up_f - field) - lower * (field - dn_f), up_f, dn_f


def stencil(state, weight, ax_halo, rad_halo, jac_radial):
    nv = state.shape[2]
    (xb, xa), (rb, ra) = ax_halo, rad_halo
    visc_ax, _, _ = viscous(state, weight, xb[:, :, :nv], xa[:, :, :nv], xb[:, :, nv:], xa[:, :, nv:], 0)
    visc_rad, up_f, dn_f = viscous(state, weight, rb[:, :, :nv], ra[:, :, :nv], rb[:, :, nv:], ra[:, :, nv:], 1)
    spread = 0.5 * (up_f - dn_f)
    mixed = jac_radial[0][None, None, :, None] * spread[:, :, 0:1]
    for k in range(1, nv):
        mixed = mixed + jac_radial[k][None, None, :, None] * spread[:, :, k:k + 1]
    return viscosity * visc_ax + (mixed + viscosity * visc_rad)


def split_bf16(x):
    t = x * 65537.0
    hi = t - (t - x)
    return hi.astype(jnp.bfloat16), (x - hi).astype(jnp.bfloat16)


def line_kernel(jac_ref, lines_ref, mats_ref, out_ref):
    S, V, XL, C = lines_ref.shape
    nx = S * XL
    cols = [lines_ref[:, v, :, :].reshape(nx, C) for v in range(V)]
    wide = jnp.concatenate(cols, axis=1)
    w_hi, w_lo = split_bf16(wide)
    m_hi, m_lo = split_bf16(mats_ref[...])
    prod = jnp.dot(m_hi, w_hi, preferred_element_type=jnp.float32)
    prod = prod + jnp.dot(m_hi, w_lo, preferred_element_type=jnp.float32)
    prod = prod + jnp.dot(m_lo, w_hi, preferred_element_type=jnp.float32)
    smooth = prod[:nx]
    slope = prod[nx:]
    for v in range(V):
        mix = jac_ref[0, v] * slope[:, 0:C]
        for k in range(1, V):
            mix = mix + jac_ref[k, v] * slope[:, k * C:(k + 1) * C]
        res = cols[v] - smooth[:, v * C:(v + 1) * C] + section_step * mix
        out_ref[:, v, :, :] = res.reshape(S, XL, C)


def line_section(lines, mats, jac_axial):
    S, V, XL, A = lines.shape
    C = 128 if A % 128 == 0 else A
    block = pl.BlockSpec((S, V, XL, C), lambda i: (0, 0, 0, i))
    whole = pl.BlockSpec(mats.shape, lambda i: (0, 0))
    return pl.pallas_call(
        line_kernel,
        out_shape=jax.ShapeDtypeStruct(lines.shape, lines.dtype),
        grid=(A // C,),
        in_specs=[pl.BlockSpec(memory_space=pltpu.SMEM), block, whole],
        out_specs=block,
        input_output_aliases={1: 0},
        compiler_params=pltpu.CompilerParams(vmem_limit_bytes=48 * 1024 * 1024),
    )(jac_axial, lines, mats)


def swap_kernel(x_ref, o_ref):
    for v in range(x_ref.shape[1]):
        o_ref[:, v, :, :] = jnp.swapaxes(x_ref[:, v, :, :], 0, 1)


def swap_outer(x):
    X, V, R, A = x.shape
    C = 128 if A % 128 == 0 else A
    return pl.pallas_call(
        swap_kernel,
        out_shape=jax.ShapeDtypeStruct((R, V, X, A), x.dtype),
        grid=(A // C,),
        in_specs=[pl.BlockSpec((X, V, R, C), lambda a: (0, 0, 0, a))],
        out_specs=pl.BlockSpec((R, V, X, C), lambda a: (0, 0, 0, a)),
        compiler_params=pltpu.CompilerParams(vmem_limit_bytes=48 * 1024 * 1024),
    )(x)


def body(state, metric, deriv, filt_corr, jac_axial, jac_radial):
    nx, nr, nv, na = state.shape
    peers = lax.axis_size("ax")
    assert nr == peers
    mats = jnp.concatenate([filt_corr, deriv], axis=0)
    weight = metric.reshape(metric.shape[0], metric.shape[1], 1, metric.shape[2])
    packed = jnp.concatenate([state, weight], axis=2)
    send = swap_outer(jnp.transpose(state, (0, 2, 1, 3)))
    lines = lax.all_to_all(send, "ax", split_axis=0, concat_axis=0, tiled=True)
    ax_halo = halos(packed, "ax", 0)
    rad_halo = halos(packed, "rad", 1)
    res = line_section(lines, mats, jac_axial)
    res, ax_halo, rad_halo = lax.optimization_barrier((res, ax_halo, rad_halo))
    ret = lax.all_to_all(res, "ax", split_axis=0, concat_axis=0, tiled=True)
    local = stencil(state, weight, ax_halo, rad_halo, jac_radial)
    local = with_layout_constraint(local, Layout(major_to_minor=(0, 2, 1, 3)))
    ret, local = lax.optimization_barrier((ret, local))
    return jnp.transpose(ret, (2, 0, 1, 3)) + section_step * local


def solution(mesh):
    in_specs = (P("ax", "rad", None, None), P("ax", "rad", None), P(), P(), P(), P())
    out_specs = P("ax", "rad", None, None)
    return jax.shard_map(body, mesh=mesh, in_specs=in_specs, out_specs=out_specs, check_vma=False)
```

```python
import functools

import jax
import jax.numpy as jnp
from jax import lax
from jax.experimental import pallas as pl
from jax.experimental.pallas import tpu as pltpu
from jax.experimental.layout import Layout, with_layout_constraint
from jax.sharding import PartitionSpec as P

section_step = 0.25
viscosity = 0.5


def halos(x, axis, dim):
    peers, length = (lax.axis_size(axis), x.shape[dim])
    up = [(i, (i + 1) % peers) for i in range(peers - 1)]
    down = [(j, i) for i, j in up]
    last = lax.slice_in_dim(x, length - 1, length, axis=dim)
    leading = lax.slice_in_dim(x, 0, 1, axis=dim)
    return lax.ppermute(last, axis, up), lax.ppermute(leading, axis, down)


def viscous(field, weight, before, after, wbefore, wafter, dim):
    up_f = jnp.concatenate([lax.slice_in_dim(field, 1, field.shape[dim], axis=dim), after], axis=dim)
    dn_f = jnp.concatenate([before, lax.slice_in_dim(field, 0, field.shape[dim] - 1, axis=dim)], axis=dim)
    up_w = jnp.concatenate([lax.slice_in_dim(weight, 1, weight.shape[dim], axis=dim), wafter], axis=dim)
    dn_w = jnp.concatenate([wbefore, lax.slice_in_dim(weight, 0, weight.shape[dim] - 1, axis=dim)], axis=dim)
    upper = 0.5 * (weight + up_w)
    lower = 0.5 * (weight + dn_w)
    return upper * (up_f - field) - lower * (field - dn_f), up_f, dn_f


def stencil(state, weight, ax_halo, rad_halo, jac_radial):
    nv = state.shape[2]
    (xb, xa), (rb, ra) = ax_halo, rad_halo
    visc_ax, _, _ = viscous(state, weight, xb[:, :, :nv], xa[:, :, :nv], xb[:, :, nv:], xa[:, :, nv:], 0)
    visc_rad, up_f, dn_f = viscous(state, weight, rb[:, :, :nv], ra[:, :, :nv], rb[:, :, nv:], ra[:, :, nv:], 1)
    spread = 0.5 * (up_f - dn_f)
    mixed = jac_radial[0][None, None, :, None] * spread[:, :, 0:1]
    for k in range(1, nv):
        mixed = mixed + jac_radial[k][None, None, :, None] * spread[:, :, k:k + 1]
    return viscosity * visc_ax + (mixed + viscosity * visc_rad)


def split_bf16(x):
    t = x * 65537.0
    hi = t - (t - x)
    return hi.astype(jnp.bfloat16), (x - hi).astype(jnp.bfloat16)


def line_kernel(jac_ref, lines_ref, mats_ref, out_ref):
    S, V, XL, C = lines_ref.shape
    nx = S * XL
    cols = [lines_ref[:, v, :, :].reshape(nx, C) for v in range(V)]
    wide = jnp.concatenate(cols, axis=1)
    w_hi, w_lo = split_bf16(wide)
    m_hi, m_lo = split_bf16(mats_ref[...])
    prod = jnp.dot(m_hi, w_hi, preferred_element_type=jnp.float32)
    prod = prod + jnp.dot(m_hi, w_lo, preferred_element_type=jnp.float32)
    prod = prod + jnp.dot(m_lo, w_hi, preferred_element_type=jnp.float32)
    smooth = prod[:nx]
    slope = prod[nx:]
    for v in range(V):
        mix = jac_ref[0, v] * slope[:, 0:C]
        for k in range(1, V):
            mix = mix + jac_ref[k, v] * slope[:, k * C:(k + 1) * C]
        res = cols[v] - smooth[:, v * C:(v + 1) * C] + section_step * mix
        out_ref[:, v, :, :] = res.reshape(S, XL, C)


def line_section(lines, mats, jac_axial):
    S, V, XL, A = lines.shape
    C = 128 if A % 128 == 0 else A
    block = pl.BlockSpec((S, V, XL, C), lambda i: (0, 0, 0, i))
    whole = pl.BlockSpec(mats.shape, lambda i: (0, 0))
    return pl.pallas_call(
        line_kernel,
        out_shape=jax.ShapeDtypeStruct(lines.shape, lines.dtype),
        grid=(A // C,),
        in_specs=[pl.BlockSpec(memory_space=pltpu.SMEM), block, whole],
        out_specs=block,
        input_output_aliases={1: 0},
        compiler_params=pltpu.CompilerParams(vmem_limit_bytes=48 * 1024 * 1024),
    )(jac_axial, lines, mats)


def swap_kernel(x_ref, o_ref):
    for v in range(x_ref.shape[1]):
        o_ref[:, v, :, :] = jnp.swapaxes(x_ref[:, v, :, :], 0, 1)


def swap_outer(x):
    X, V, R, A = x.shape
    C = 128 if A % 128 == 0 else A
    return pl.pallas_call(
        swap_kernel,
        out_shape=jax.ShapeDtypeStruct((R, V, X, A), x.dtype),
        grid=(A // C,),
        in_specs=[pl.BlockSpec((X, V, R, C), lambda a: (0, 0, 0, a))],
        out_specs=pl.BlockSpec((R, V, X, C), lambda a: (0, 0, 0, a)),
        compiler_params=pltpu.CompilerParams(vmem_limit_bytes=48 * 1024 * 1024),
    )(x)


def finish_kernel(ret_ref, local_ref, o_ref):
    for v in range(ret_ref.shape[1]):
        o_ref[:, v, :, :] = jnp.swapaxes(ret_ref[:, v, :, :], 0, 1) + section_step * local_ref[:, v, :, :]


def finish(ret, local_t):
    R, V, X, A = ret.shape
    C = 128 if A % 128 == 0 else A
    return pl.pallas_call(
        finish_kernel,
        out_shape=jax.ShapeDtypeStruct(local_t.shape, local_t.dtype),
        grid=(A // C,),
        in_specs=[
            pl.BlockSpec((R, V, X, C), lambda a: (0, 0, 0, a)),
            pl.BlockSpec((X, V, R, C), lambda a: (0, 0, 0, a)),
        ],
        out_specs=pl.BlockSpec((X, V, R, C), lambda a: (0, 0, 0, a)),
        compiler_params=pltpu.CompilerParams(vmem_limit_bytes=48 * 1024 * 1024),
    )(ret, local_t)


def body(state, metric, deriv, filt_corr, jac_axial, jac_radial):
    nx, nr, nv, na = state.shape
    peers = lax.axis_size("ax")
    assert nr == peers
    mats = jnp.concatenate([filt_corr, deriv], axis=0)
    weight = metric.reshape(metric.shape[0], metric.shape[1], 1, metric.shape[2])
    packed = jnp.concatenate([state, weight], axis=2)
    send = swap_outer(jnp.transpose(state, (0, 2, 1, 3)))
    lines = lax.all_to_all(send, "ax", split_axis=0, concat_axis=0, tiled=True)
    ax_halo = halos(packed, "ax", 0)
    rad_halo = halos(packed, "rad", 1)
    res = line_section(lines, mats, jac_axial)
    res, ax_halo, rad_halo = lax.optimization_barrier((res, ax_halo, rad_halo))
    ret = lax.all_to_all(res, "ax", split_axis=0, concat_axis=0, tiled=True)
    local = stencil(state, weight, ax_halo, rad_halo, jac_radial)
    local = with_layout_constraint(local, Layout(major_to_minor=(0, 2, 1, 3)))
    ret, local = lax.optimization_barrier((ret, local))
    out = finish(ret, jnp.transpose(local, (0, 2, 1, 3)))
    return jnp.transpose(out, (0, 2, 1, 3))


def solution(mesh):
    in_specs = (P("ax", "rad", None, None), P("ax", "rad", None), P(), P(), P(), P())
    out_specs = P("ax", "rad", None, None)
    return jax.shard_map(body, mesh=mesh, in_specs=in_specs, out_specs=out_specs, check_vma=False)
```

```python
import functools

import jax
import jax.numpy as jnp
from jax import lax
from jax.experimental import pallas as pl
from jax.experimental.pallas import tpu as pltpu
from jax.experimental.layout import Layout, with_layout_constraint
from jax.sharding import PartitionSpec as P

section_step = 0.25
viscosity = 0.5


def halos(x, axis, dim):
    peers, length = (lax.axis_size(axis), x.shape[dim])
    up = [(i, (i + 1) % peers) for i in range(peers - 1)]
    down = [(j, i) for i, j in up]
    last = lax.slice_in_dim(x, length - 1, length, axis=dim)
    leading = lax.slice_in_dim(x, 0, 1, axis=dim)
    return lax.ppermute(last, axis, up), lax.ppermute(leading, axis, down)


def viscous(field, weight, before, after, wbefore, wafter, dim):
    up_f = jnp.concatenate([lax.slice_in_dim(field, 1, field.shape[dim], axis=dim), after], axis=dim)
    dn_f = jnp.concatenate([before, lax.slice_in_dim(field, 0, field.shape[dim] - 1, axis=dim)], axis=dim)
    up_w = jnp.concatenate([lax.slice_in_dim(weight, 1, weight.shape[dim], axis=dim), wafter], axis=dim)
    dn_w = jnp.concatenate([wbefore, lax.slice_in_dim(weight, 0, weight.shape[dim] - 1, axis=dim)], axis=dim)
    upper = 0.5 * (weight + up_w)
    lower = 0.5 * (weight + dn_w)
    return upper * (up_f - field) - lower * (field - dn_f), up_f, dn_f


def stencil(state, weight, ax_halo, rad_halo, jac_radial):
    nv = state.shape[2]
    (xb, xa), (rb, ra) = ax_halo, rad_halo
    visc_ax, _, _ = viscous(state, weight, xb[:, :, :nv], xa[:, :, :nv], xb[:, :, nv:], xa[:, :, nv:], 0)
    visc_rad, up_f, dn_f = viscous(state, weight, rb[:, :, :nv], ra[:, :, :nv], rb[:, :, nv:], ra[:, :, nv:], 1)
    spread = 0.5 * (up_f - dn_f)
    mixed = jac_radial[0][None, None, :, None] * spread[:, :, 0:1]
    for k in range(1, nv):
        mixed = mixed + jac_radial[k][None, None, :, None] * spread[:, :, k:k + 1]
    return viscosity * visc_ax + (mixed + viscosity * visc_rad)


def split_bf16(x):
    t = x * 65537.0
    hi = t - (t - x)
    return hi.astype(jnp.bfloat16), (x - hi).astype(jnp.bfloat16)


def split_kernel(m_ref, hi_ref, lo_ref):
    hi, lo = split_bf16(m_ref[...])
    hi_ref[...] = hi
    lo_ref[...] = lo


def split_mats(mats):
    part = jax.ShapeDtypeStruct(mats.shape, jnp.bfloat16)
    return pl.pallas_call(split_kernel, out_shape=(part, part))(mats)


def line_kernel(jac_ref, lines_ref, hi_ref, lo_ref, out_ref):
    S, V, XL, C = lines_ref.shape
    nx = S * XL
    cols = [lines_ref[:, v, :, :].reshape(nx, C) for v in range(V)]
    wide = jnp.concatenate(cols, axis=1)
    w_hi, w_lo = split_bf16(wide)
    m_hi = hi_ref[...]
    m_lo = lo_ref[...]
    prod = jnp.dot(m_hi, w_hi, preferred_element_type=jnp.float32)
    prod = prod + jnp.dot(m_hi, w_lo, preferred_element_type=jnp.float32)
    prod = prod + jnp.dot(m_lo, w_hi, preferred_element_type=jnp.float32)
    smooth = prod[:nx]
    slope = prod[nx:]
    for v in range(V):
        mix = jac_ref[0, v] * slope[:, 0:C]
        for k in range(1, V):
            mix = mix + jac_ref[k, v] * slope[:, k * C:(k + 1) * C]
        res = cols[v] - smooth[:, v * C:(v + 1) * C] + section_step * mix
        out_ref[:, v, :, :] = res.reshape(S, XL, C)


def line_section(lines, mats, jac_axial):
    S, V, XL, A = lines.shape
    C = 128 if A % 128 == 0 else A
    block = pl.BlockSpec((S, V, XL, C), lambda i: (0, 0, 0, i))
    whole = pl.BlockSpec(mats.shape, lambda i: (0, 0))
    return pl.pallas_call(
        line_kernel,
        out_shape=jax.ShapeDtypeStruct(lines.shape, lines.dtype),
        grid=(A // C,),
        in_specs=[pl.BlockSpec(memory_space=pltpu.SMEM), block, whole, whole],
        out_specs=block,
        input_output_aliases={1: 0},
        compiler_params=pltpu.CompilerParams(vmem_limit_bytes=48 * 1024 * 1024),
    )(jac_axial, lines, *split_mats(mats))


def swap_kernel(x_ref, o_ref):
    for v in range(x_ref.shape[1]):
        o_ref[:, v, :, :] = jnp.swapaxes(x_ref[:, v, :, :], 0, 1)


def swap_outer(x):
    X, V, R, A = x.shape
    C = 128 if A % 128 == 0 else A
    return pl.pallas_call(
        swap_kernel,
        out_shape=jax.ShapeDtypeStruct((R, V, X, A), x.dtype),
        grid=(A // C,),
        in_specs=[pl.BlockSpec((X, V, R, C), lambda a: (0, 0, 0, a))],
        out_specs=pl.BlockSpec((R, V, X, C), lambda a: (0, 0, 0, a)),
        compiler_params=pltpu.CompilerParams(vmem_limit_bytes=48 * 1024 * 1024),
    )(x)


def finish_kernel(ret_ref, local_ref, o_ref):
    for v in range(ret_ref.shape[1]):
        o_ref[:, v, :, :] = jnp.swapaxes(ret_ref[:, v, :, :], 0, 1) + section_step * local_ref[:, v, :, :]


def finish(ret, local_t):
    R, V, X, A = ret.shape
    C = 128 if A % 128 == 0 else A
    return pl.pallas_call(
        finish_kernel,
        out_shape=jax.ShapeDtypeStruct(local_t.shape, local_t.dtype),
        grid=(A // C,),
        in_specs=[
            pl.BlockSpec((R, V, X, C), lambda a: (0, 0, 0, a)),
            pl.BlockSpec((X, V, R, C), lambda a: (0, 0, 0, a)),
        ],
        out_specs=pl.BlockSpec((X, V, R, C), lambda a: (0, 0, 0, a)),
        compiler_params=pltpu.CompilerParams(vmem_limit_bytes=48 * 1024 * 1024),
    )(ret, local_t)


def body(state, metric, deriv, filt_corr, jac_axial, jac_radial):
    nx, nr, nv, na = state.shape
    peers = lax.axis_size("ax")
    assert nr == peers
    mats = jnp.concatenate([filt_corr, deriv], axis=0)
    weight = metric.reshape(metric.shape[0], metric.shape[1], 1, metric.shape[2])
    packed = jnp.concatenate([state, weight], axis=2)
    send = swap_outer(jnp.transpose(state, (0, 2, 1, 3)))
    lines = lax.all_to_all(send, "ax", split_axis=0, concat_axis=0, tiled=True)
    ax_halo = halos(packed, "ax", 0)
    rad_halo = halos(packed, "rad", 1)
    res = line_section(lines, mats, jac_axial)
    res, ax_halo, rad_halo = lax.optimization_barrier((res, ax_halo, rad_halo))
    ret = lax.all_to_all(res, "ax", split_axis=0, concat_axis=0, tiled=True)
    local = stencil(state, weight, ax_halo, rad_halo, jac_radial)
    local = with_layout_constraint(local, Layout(major_to_minor=(0, 2, 1, 3)))
    ret, local = lax.optimization_barrier((ret, local))
    out = finish(ret, jnp.transpose(local, (0, 2, 1, 3)))
    return jnp.transpose(out, (0, 2, 1, 3))


def solution(mesh):
    in_specs = (P("ax", "rad", None, None), P("ax", "rad", None), P(), P(), P(), P())
    out_specs = P("ax", "rad", None, None)
    return jax.shard_map(body, mesh=mesh, in_specs=in_specs, out_specs=out_specs, check_vma=False)
```
